256 devices in a mesh: feat: 64 (over x, z, core), rep: 4 (over y).
Axes of the slice: x: 4, y: 4, z: 8, core: 2. Of those that a mesh axis runs over, the one named last changes fastest.
Arguments:
- features: bfloat16 [4, 128, 32768], P('rep', 'feat'), may hold values from -6 to 6
- neighbors_one: int32 [4, 15, 16384], P('rep'), may hold values from 0 to 32767, as said below
- weight_one: bfloat16 [2, 128, 256], P(None, 'feat'), may hold values from -0.375 to 0.375
- weight_two: bfloat16 [2, 256, 256], replicated, may hold values from -0.25 to 0.25
- send_rows: int32 [4, 64, 64, 32], P('rep', 'feat'), may hold values from 0 to 255
- halo_count: int32 [4, 64, 64], P('rep', 'feat'), may hold values from 1 to 32, as said below
- neighbors_two: int32 [4, 10, 16384], P('rep', None, 'feat'), may hold values from 0 to 2303, as said below
- cotangent: bfloat16 [4, 16384, 256], P('rep', 'feat'), may hold values from -6 to 6
Outputs:
- hidden_two: bfloat16 [4, 16384, 256], P('rep', 'feat')
- grad_one: float32 [2, 128, 256], P(None, 'feat')
- grad_two: float32 [2, 256, 256], replicated
The draws below stay inside these ranges and needn't reach their ends.
Inputs may be any that keep to these rules, and one draw needn't show every extreme that they name: neighbors_one[r, k, v] lies in the block of sources from 2 * 512 * (v // 512) to 2 * 512 * (v // 512) + 2 * 512 - 1. halo_count[r, p, q] is how many halo slots shard p fills for shard q; in every replica one shard q receives exactly 32 from every shard, every other count is at most 24. send_rows[r, p, q, j] is a local row of shard p; entries with j >= halo_count[r, p, q] are ignored. `neighbors_two`: an entry below 256 is a local row; an entry 256 + p * 32 + j is a halo slot with j < halo_count[r, p, q] for the seed's shard q; every such live slot is named at least once on its shard.
All inputs are finite; a program needn't handle non-finite values.
Results may differ from the reference program's by a relative error of at most 0.0051.
Values may be sent and summed in bfloat16 or wider, within the bound.
No kernel may reach another device: no remote copies, remote signals or barrier semaphores. Data moves between devices by JAX's collectives and lax.ppermute only.
A program may use at most 64 MiB of HBM per device.

```python
import math
import jax
import jax.numpy as jnp
from jax import lax

FEATS = 128
UNITS = 256
FANOUT_ONE = 15
FANOUT_TWO = 10
BLOCK_NODES = 512
NODES_DEV = 256
SEEDS_DEV = 256
CAP = 32
REPLICAS = 4
SHARDS = 64
LAYER_ONE = 16384
SOURCES = 32768
SEEDS = 16384


def draw_neighbors_one(key, part):
    own_key = jax.random.fold_in(key, 29)
    offsets = jax.random.randint(own_key, (REPLICAS, FANOUT_ONE, LAYER_ONE), 0, 2 * BLOCK_NODES)
    node_index = jnp.arange(LAYER_ONE, dtype=jnp.int32)
    base = node_index // BLOCK_NODES * (2 * BLOCK_NODES)
    return (offsets + base[None, None, :]).astype(jnp.int32)


def halo_plan(key):
    base_key = jax.random.fold_in(key, 7)
    first_key, second_key = jax.random.split(base_key)
    counts = jax.random.randint(first_key, (REPLICAS, SHARDS, SHARDS), 1, 3 * CAP // 4 + 1)
    heavy_peer = jax.random.randint(second_key, (REPLICAS, 1, 1), 0, SHARDS)
    column = jnp.arange(SHARDS, dtype=jnp.int32)[None, None, :]
    return jnp.where(column == heavy_peer, CAP, counts).astype(jnp.int32)


def draw_halo_count(key, part):
    return halo_plan(key)


def one_device(device_key, column_counts):
    slot_total = SHARDS * CAP
    ref_total = FANOUT_TWO * SEEDS_DEV
    extra_refs = ref_total - slot_total
    draw_keys = jax.random.split(device_key, 5)
    slot_index = jnp.arange(slot_total, dtype=jnp.int32)
    live_slots = slot_index % CAP < column_counts[slot_index // CAP]
    local_first = jax.random.randint(draw_keys[0], (slot_total,), 0, NODES_DEV)
    first_part = jnp.where(live_slots, NODES_DEV + slot_index, local_first)
    picked = jax.random.randint(draw_keys[1], (extra_refs,), 0, slot_total)
    coin_flip = jax.random.randint(draw_keys[2], (extra_refs,), 0, 2)
    local_rest = jax.random.randint(draw_keys[3], (extra_refs,), 0, NODES_DEV)
    rest_part = jnp.where((coin_flip == 1) & live_slots[picked], NODES_DEV + picked, local_rest)
    merged = jnp.concatenate([first_part, rest_part])
    shuffle = jax.random.permutation(draw_keys[4], ref_total)
    return merged[shuffle].reshape(FANOUT_TWO, SEEDS_DEV)


def draw_neighbors_two(key, part):
    counts = halo_plan(key)
    ref_key = jax.random.fold_in(key, 13)
    per_counts = jnp.swapaxes(counts, 1, 2).reshape(REPLICAS * SHARDS, SHARDS)
    flat_index = jnp.arange(REPLICAS * SHARDS, dtype=jnp.int32)

    def device_draw(device_number, column_counts):
        return one_device(jax.random.fold_in(ref_key, device_number), column_counts)
    drawn_refs = jax.vmap(device_draw)(flat_index, per_counts)
    drawn_refs = drawn_refs.reshape(REPLICAS, SHARDS, FANOUT_TWO, SEEDS_DEV)
    return jnp.transpose(drawn_refs, (0, 2, 1, 3)).reshape(REPLICAS, FANOUT_TWO, SHARDS * SEEDS_DEV).astype(jnp.int32)


def place_ends(drawn, stream_key, smallest, largest):
    longest = drawn.shape.index(max(drawn.shape))
    spots = []
    for shift in (0, 1):
        where = [jax.random.randint(jax.random.fold_in(stream_key, axis), (), 0, length) for axis, length in enumerate(drawn.shape)]
        where[longest] = (where[longest] + shift) % drawn.shape[longest]
        spots.append(tuple(where))
    return drawn.at[spots[0]].set(smallest).at[spots[1]].set(largest)


def level_of(stream_key, extent, shards, least, largest):
    loudness = 1.0
    for dim, blocks in shards:
        heights = jax.random.uniform(jax.random.fold_in(jax.random.fold_in(stream_key, 6), dim), (blocks,), jnp.float32, least / len(shards), largest / len(shards))
        loudness = loudness * jnp.repeat(jnp.exp(heights), extent[dim] // blocks).reshape((-1,) + (1,) * (len(extent) - 1 - dim))
    return loudness


def centred(key, dims, deviation, limit, pieces=(), kind=jnp.bfloat16):
    result = jax.random.normal(key, dims, jnp.float32) * deviation
    if len(pieces) > 0:
        result = level_of(key, dims, pieces, -0.22, 0.18) * result
    return jnp.clip(result, min=-limit, max=limit).astype(kind)


def setup_inputs(seed: int = 0) -> dict:
    keys = jax.random.split(jax.random.key(seed), 9)
    return {
        "features": centred(keys[0], (REPLICAS, FEATS, SOURCES), 1.0, 6.0, ((0, 4), (1, 64))),
        "neighbors_one": draw_neighbors_one(jax.random.fold_in(keys[8], 71), 0),
        "weight_one": centred(keys[2], (2, FEATS, UNITS), (2 * FEATS) ** -0.5, 0.375, ((1, 64),)),
        "weight_two": centred(keys[3], (2, UNITS, UNITS), (2 * UNITS) ** -0.5, 0.25),
        "send_rows": place_ends(jax.random.randint(keys[4], (REPLICAS, SHARDS, SHARDS, CAP), 0, NODES_DEV), jax.random.fold_in(keys[4], 1), 0, NODES_DEV - 1).astype(jnp.int32),
        "halo_count": draw_halo_count(jax.random.fold_in(keys[8], 71), 0),
        "neighbors_two": draw_neighbors_two(jax.random.fold_in(keys[8], 71), 0),
        "cotangent": centred(keys[7], (REPLICAS, SEEDS, UNITS), 1.0, 6.0, ((0, 4), (1, 64))),
    }


def activate(pre):
    return jnp.where(pre > 0.0, pre, jnp.expm1(jnp.minimum(pre, 0.0)))

def elu_slope(pre):
    return jnp.where(pre > 0.0, jnp.ones_like(pre), jnp.exp(jnp.minimum(pre, 0.0)))

def product(left, right):
    return jnp.dot(left.astype(jnp.float32), right.astype(jnp.float32), precision=lax.Precision.HIGHEST)

def reference(features, neighbors_one, weight_one, weight_two, send_rows, halo_count, neighbors_two, cotangent):
    grad_scale = 1.0 / math.sqrt(REPLICAS * SEEDS)
    peer_index = jnp.arange(SHARDS, dtype=jnp.int32)
    slot_index = jnp.arange(CAP, dtype=jnp.int32)

    def one_replica(carry, inputs):
        grad_one, grad_two = carry
        table_x, index_one, send_slots, counts, index_flat, cot = inputs
        summed = jnp.zeros((FEATS, LAYER_ONE), jnp.float32)
        for sample in range(FANOUT_ONE):
            summed = summed + jnp.take(table_x, index_one[sample], axis=1).astype(jnp.float32)
        aggregate_one = (summed / FANOUT_ONE).astype(jnp.bfloat16)
        self_one = table_x[:, :LAYER_ONE]
        pre_one = product(self_one.T, weight_one[0]) + product(aggregate_one.T, weight_one[1])
        hidden_one = activate(pre_one).astype(jnp.bfloat16)
        blocks = hidden_one.reshape(SHARDS, NODES_DEV, UNITS)
        live_slots = slot_index[None, None, :] < counts[:, :, None]
        sent_rows = blocks[peer_index[:, None, None], send_slots]
        sent_rows = jnp.where(live_slots[:, :, :, None], sent_rows, jnp.zeros_like(sent_rows))
        received = jnp.swapaxes(sent_rows, 0, 1).reshape(SHARDS, SHARDS * CAP, UNITS)
        tables = jnp.concatenate([blocks, received], axis=1)
        index_two = index_flat.reshape(FANOUT_TWO, SHARDS, SEEDS_DEV)
        summed_two = jnp.zeros((SHARDS, SEEDS_DEV, UNITS), jnp.float32)
        for sample in range(FANOUT_TWO):
            summed_two = summed_two + tables[peer_index[:, None], index_two[sample]].astype(jnp.float32)
        aggregate_two = (summed_two / FANOUT_TWO).astype(jnp.bfloat16).reshape(SEEDS, UNITS)
        self_two = blocks[:, :SEEDS_DEV].reshape(SEEDS, UNITS)
        pre_two = product(self_two, weight_two[0]) + product(aggregate_two, weight_two[1])
        hidden_two = activate(pre_two).astype(jnp.bfloat16)
        slope_two = (cot.astype(jnp.float32) * elu_slope(pre_two) * grad_scale).astype(jnp.bfloat16)
        grad_two = grad_two + jnp.stack([product(self_two.T, slope_two), product(aggregate_two.T, slope_two)])
        back_self = product(slope_two, weight_two[0].T).reshape(SHARDS, SEEDS_DEV, UNITS)
        back_agg = (product(slope_two, weight_two[1].T) / FANOUT_TWO).reshape(SHARDS, SEEDS_DEV, UNITS)
        grad_tables = jnp.zeros((SHARDS, NODES_DEV + SHARDS * CAP, UNITS), jnp.float32)
        for sample in range(FANOUT_TWO):
            grad_tables = grad_tables.at[peer_index[:, None], index_two[sample]].add(back_agg)
        grad_tables = grad_tables.at[:, :SEEDS_DEV].add(back_self)
        returned = jnp.swapaxes(grad_tables[:, NODES_DEV:].reshape(SHARDS, SHARDS, CAP, UNITS), 0, 1)
        returned = jnp.where(live_slots[:, :, :, None], returned, jnp.zeros_like(returned))
        back_one = grad_tables[:, :NODES_DEV].at[peer_index[:, None, None], send_slots].add(returned)
        slope_one = (back_one.reshape(LAYER_ONE, UNITS) * elu_slope(pre_one)).astype(jnp.bfloat16)
        grad_one = grad_one + jnp.stack([product(self_one, slope_one), product(aggregate_one, slope_one)])
        return ((grad_one, grad_two), hidden_two)
    start = (jnp.zeros((2, FEATS, UNITS), jnp.float32), jnp.zeros((2, UNITS, UNITS), jnp.float32))
    (grad_one, grad_two), layer_two = lax.scan(one_replica, start, (features, neighbors_one, send_rows, halo_count, neighbors_two, cotangent))
    return (layer_two, grad_one, grad_two)
```

```python
import math

import jax
import jax.numpy as jnp
from jax import lax
from jax.sharding import PartitionSpec as P

BLOCK_NODES = 512


def activate(pre):
    return jnp.where(pre > 0.0, pre, jnp.expm1(jnp.minimum(pre, 0.0)))


def elu_slope(pre):
    return jnp.where(pre > 0.0, jnp.ones_like(pre), jnp.exp(jnp.minimum(pre, 0.0)))


def on_device(
    features, neighbors_one, weight_one, weight_two, send_rows, halo_count, neighbors_two, cotangent
):
    feat_devs = lax.axis_size("feat")
    rep_devs = lax.axis_size("rep")
    me = lax.axis_index("feat")
    table_x = features[0]
    cols_dev, sources = table_x.shape
    index_one = neighbors_one[0]
    fanout_one, layer_rows = index_one.shape
    node_count = layer_rows // feat_devs
    hidden_width = weight_one.shape[2]
    span_width = 2 * BLOCK_NODES
    span_count = sources // span_width
    nodes_per_span = BLOCK_NODES // node_count

    block_part = jnp.repeat(
        jnp.transpose(table_x.reshape(cols_dev, span_count, span_width), (1, 0, 2)),
        nodes_per_span,
        axis=0,
    )[: feat_devs]
    self_part = jnp.transpose(
        table_x[:, :layer_rows].reshape(cols_dev, feat_devs, node_count), (1, 0, 2)
    )
    weight_part = jnp.transpose(weight_one, (1, 0, 2)).reshape(cols_dev, 2 * hidden_width)
    weight_part = jnp.broadcast_to(weight_part[None], (feat_devs, cols_dev, 2 * hidden_width))
    outgoing_one = jnp.concatenate([block_part, self_part, weight_part], axis=2)
    incoming_one = lax.all_to_all(outgoing_one, "feat", split_axis=0, concat_axis=0, tiled=True)
    gathered = incoming_one.reshape(feat_devs * cols_dev, -1)
    block_x = gathered[:, :span_width]
    self_x = gathered[:, span_width : span_width + node_count]
    full_weight = gathered[:, span_width + node_count :].reshape(-1, 2, hidden_width)

    my_index = lax.dynamic_slice_in_dim(index_one, me * node_count, node_count, axis=1)
    block_start = (me * node_count) // BLOCK_NODES * span_width
    relative = my_index - block_start
    positions = lax.broadcasted_iota(jnp.int32, (node_count, span_width), 1)
    tallies = jnp.zeros((node_count, span_width), jnp.float32)
    for sample in range(fanout_one):
        tallies = tallies + (relative[sample][:, None] == positions).astype(jnp.float32)
    tallies = tallies.astype(jnp.bfloat16)
    summed_one = jnp.einsum("fs,vs->fv", block_x, tallies, preferred_element_type=jnp.float32)
    aggregate_one = (summed_one / fanout_one).astype(jnp.bfloat16)

    pre_one = jnp.einsum(
        "fv,fh->vh", self_x, full_weight[:, 0], preferred_element_type=jnp.float32
    ) + jnp.einsum("fv,fh->vh", aggregate_one, full_weight[:, 1], preferred_element_type=jnp.float32)
    hidden_one = activate(pre_one).astype(jnp.bfloat16)

    send_slots = send_rows[0, 0]
    counts = halo_count[0, 0]
    capacity = send_slots.shape[1]
    live_slots = lax.broadcasted_iota(jnp.int32, send_slots.shape, 1) < counts[:, None]
    outgoing = jnp.where(
        live_slots[:, :, None], hidden_one[send_slots], jnp.zeros((), jnp.bfloat16)
    )
    incoming = lax.all_to_all(outgoing, "feat", split_axis=0, concat_axis=0, tiled=True)
    table_two = jnp.concatenate(
        [hidden_one, incoming.reshape(feat_devs * capacity, hidden_width)], axis=0
    )
    index_two = neighbors_two[0]
    fanout_two = index_two.shape[0]
    seed_rows = index_two.shape[1]
    summed_two = jnp.zeros((seed_rows, hidden_width), jnp.float32)
    for sample in range(fanout_two):
        summed_two = summed_two + table_two[index_two[sample]].astype(jnp.float32)
    aggregate_two = (summed_two / fanout_two).astype(jnp.bfloat16)
    pre_two = jnp.dot(hidden_one, weight_two[0], preferred_element_type=jnp.float32) + jnp.dot(
        aggregate_two, weight_two[1], preferred_element_type=jnp.float32
    )
    hidden_two = activate(pre_two).astype(jnp.bfloat16)
    grad_scale = 1.0 / math.sqrt(rep_devs * feat_devs * seed_rows)
    slope_two = (cotangent[0].astype(jnp.float32) * elu_slope(pre_two) * grad_scale).astype(
        jnp.bfloat16
    )
    local_two = jnp.stack(
        [
            jnp.einsum("rh,rk->hk", hidden_one, slope_two, preferred_element_type=jnp.float32),
            jnp.einsum("rh,rk->hk", aggregate_two, slope_two, preferred_element_type=jnp.float32),
        ]
    )
    back_self = jnp.einsum(
        "rk,hk->rh", slope_two, weight_two[0], preferred_element_type=jnp.float32
    )
    back_agg = (
        jnp.einsum("rk,hk->rh", slope_two, weight_two[1], preferred_element_type=jnp.float32)
        / fanout_two
    )
    grad_table = jnp.zeros((table_two.shape[0], hidden_width), jnp.float32)
    for sample in range(fanout_two):
        grad_table = grad_table.at[index_two[sample]].add(back_agg)
    grad_table = grad_table.at[:seed_rows].add(back_self)
    returned = lax.all_to_all(
        grad_table[node_count:].reshape(feat_devs, capacity, hidden_width).astype(jnp.bfloat16),
        "feat",
        split_axis=0,
        concat_axis=0,
        tiled=True,
    ).astype(jnp.float32)
    returned = jnp.where(live_slots[:, :, None], returned, 0.0)
    back_one = grad_table[:node_count].at[send_slots].add(returned)
    slope_one = (back_one * elu_slope(pre_one)).astype(jnp.bfloat16)
    local_one = jnp.stack(
        [
            jnp.einsum("fv,vh->fh", self_x, slope_one, preferred_element_type=jnp.float32),
            jnp.einsum("fv,vh->fh", aggregate_one, slope_one, preferred_element_type=jnp.float32),
        ]
    )

    one_part = jnp.transpose(
        local_one.reshape(2, feat_devs, cols_dev, hidden_width), (1, 0, 2, 3)
    ).reshape(feat_devs, -1)
    two_part = local_two.reshape(feat_devs, -1)
    outgoing_grad = jnp.concatenate([one_part, two_part], axis=1)
    incoming_grad = lax.all_to_all(outgoing_grad, "feat", split_axis=0, concat_axis=0, tiled=True)
    reduced = lax.psum(jnp.sum(incoming_grad, axis=0), "rep")
    one_size = one_part.shape[1]
    grad_one = reduced[:one_size].reshape(2, cols_dev, hidden_width)
    grad_two = lax.all_gather(reduced[one_size:], "feat", axis=0, tiled=True).reshape(
        local_two.shape
    )
    return (hidden_two[None], grad_one, grad_two)


def solution(mesh):
    return jax.shard_map(
        on_device,
        mesh=mesh,
        in_specs=(
            P("rep", "feat", None),
            P("rep", None, None),
            P(None, "feat", None),
            P(),
            P("rep", "feat", None, None),
            P("rep", "feat", None),
            P("rep", None, "feat"),
            P("rep", "feat", None),
        ),
        out_specs=(P("rep", "feat", None), P(None, "feat", None), P()),
        check_vma=False,
    )
```

```python
import math

import jax
import jax.numpy as jnp
from jax import lax
from jax.sharding import PartitionSpec as P

BLOCK_NODES = 512


def activate(pre):
    return jnp.where(pre > 0.0, pre, jnp.expm1(jnp.minimum(pre, 0.0)))


def elu_slope(pre):
    return jnp.where(pre > 0.0, jnp.ones_like(pre), jnp.exp(jnp.minimum(pre, 0.0)))


def on_device(
    features, neighbors_one, weight_one, weight_two, send_rows, halo_count, neighbors_two, cotangent
):
    feat_devs = lax.axis_size("feat")
    rep_devs = lax.axis_size("rep")
    me = lax.axis_index("feat")
    table_x = features[0]
    cols_dev, sources = table_x.shape
    index_one = neighbors_one[0]
    fanout_one, layer_rows = index_one.shape
    node_count = layer_rows // feat_devs
    hidden_width = weight_one.shape[2]
    span_width = 2 * BLOCK_NODES
    span_count = sources // span_width
    nodes_per_span = BLOCK_NODES // node_count

    block_part = jnp.repeat(
        jnp.transpose(table_x.reshape(cols_dev, span_count, span_width), (1, 0, 2)),
        nodes_per_span,
        axis=0,
    )[: feat_devs]
    self_part = jnp.transpose(
        table_x[:, :layer_rows].reshape(cols_dev, feat_devs, node_count), (1, 0, 2)
    )
    weight_part = jnp.transpose(weight_one, (1, 0, 2)).reshape(cols_dev, 2 * hidden_width)
    weight_part = jnp.broadcast_to(weight_part[None], (feat_devs, cols_dev, 2 * hidden_width))
    outgoing_one = jnp.concatenate([block_part, self_part, weight_part], axis=2)
    incoming_one = lax.all_to_all(outgoing_one, "feat", split_axis=0, concat_axis=0, tiled=True)
    gathered = incoming_one.reshape(feat_devs * cols_dev, -1)
    block_x = gathered[:, :span_width]
    self_x = gathered[:, span_width : span_width + node_count]
    full_weight = gathered[:, span_width + node_count :].reshape(-1, 2, hidden_width)

    my_index = lax.dynamic_slice_in_dim(index_one, me * node_count, node_count, axis=1)
    block_start = (me * node_count) // BLOCK_NODES * span_width
    relative = my_index - block_start
    positions = lax.broadcasted_iota(jnp.int32, (node_count, span_width), 1)
    tallies = jnp.zeros((node_count, span_width), jnp.float32)
    for sample in range(fanout_one):
        tallies = tallies + (relative[sample][:, None] == positions).astype(jnp.float32)
    tallies = tallies.astype(jnp.bfloat16)
    summed_one = jnp.einsum("fs,vs->fv", block_x, tallies, preferred_element_type=jnp.float32)
    aggregate_one = (summed_one / fanout_one).astype(jnp.bfloat16)

    pre_one = jnp.einsum(
        "fv,fh->vh", self_x, full_weight[:, 0], preferred_element_type=jnp.float32
    ) + jnp.einsum("fv,fh->vh", aggregate_one, full_weight[:, 1], preferred_element_type=jnp.float32)
    hidden_one = activate(pre_one).astype(jnp.bfloat16)

    send_slots = send_rows[0, 0]
    counts = halo_count[0, 0]
    peers, capacity = send_slots.shape
    live_slots = lax.broadcasted_iota(jnp.int32, send_slots.shape, 1) < counts[:, None]
    local_rows = lax.broadcasted_iota(jnp.int32, (peers, capacity, node_count), 2)
    picks = ((send_slots[:, :, None] == local_rows) & live_slots[:, :, None]).astype(jnp.bfloat16)
    picks = picks.reshape(peers * capacity, node_count)
    outgoing = jnp.einsum(
        "ji,ih->jh", picks, hidden_one, preferred_element_type=jnp.float32
    ).astype(jnp.bfloat16)
    incoming = lax.all_to_all(
        outgoing.reshape(peers, capacity, hidden_width), "feat", split_axis=0, concat_axis=0, tiled=True
    )
    table_two = jnp.concatenate(
        [hidden_one, incoming.reshape(feat_devs * capacity, hidden_width)], axis=0
    )
    index_two = neighbors_two[0]
    fanout_two = index_two.shape[0]
    seed_rows = index_two.shape[1]
    table_rows = table_two.shape[0]
    rows_two = lax.broadcasted_iota(jnp.int32, (seed_rows, table_rows), 1)
    tallies_two = jnp.zeros((seed_rows, table_rows), jnp.float32)
    for sample in range(fanout_two):
        tallies_two = tallies_two + (index_two[sample][:, None] == rows_two).astype(jnp.float32)
    summed_two = jnp.einsum(
        "dr,rh->dh", tallies_two.astype(jnp.bfloat16), table_two, preferred_element_type=jnp.float32
    )
    aggregate_two = (summed_two / fanout_two).astype(jnp.bfloat16)
    pre_two = jnp.dot(hidden_one, weight_two[0], preferred_element_type=jnp.float32) + jnp.dot(
        aggregate_two, weight_two[1], preferred_element_type=jnp.float32
    )
    hidden_two = activate(pre_two).astype(jnp.bfloat16)
    grad_scale = 1.0 / math.sqrt(rep_devs * feat_devs * seed_rows)
    slope_two = (cotangent[0].astype(jnp.float32) * elu_slope(pre_two) * grad_scale).astype(
        jnp.bfloat16
    )
    local_two = jnp.stack(
        [
            jnp.einsum("rh,rk->hk", hidden_one, slope_two, preferred_element_type=jnp.float32),
            jnp.einsum("rh,rk->hk", aggregate_two, slope_two, preferred_element_type=jnp.float32),
        ]
    )
    back_self = jnp.einsum(
        "rk,hk->rh", slope_two, weight_two[0], preferred_element_type=jnp.float32
    )
    back_agg = (
        jnp.einsum("rk,hk->rh", slope_two, weight_two[1], preferred_element_type=jnp.float32)
        / fanout_two
    )
    grad_table = jnp.einsum(
        "dr,dh->rh", tallies_two, back_agg, precision=lax.Precision.HIGHEST,
        preferred_element_type=jnp.float32,
    )
    returned = lax.all_to_all(
        grad_table[node_count:].reshape(peers, capacity, hidden_width).astype(jnp.bfloat16),
        "feat",
        split_axis=0,
        concat_axis=0,
        tiled=True,
    )
    back_one = grad_table[:node_count] + back_self + jnp.einsum(
        "ji,jh->ih", picks, returned.reshape(peers * capacity, hidden_width),
        preferred_element_type=jnp.float32,
    )
    slope_one = (back_one * elu_slope(pre_one)).astype(jnp.bfloat16)
    local_one = jnp.stack(
        [
            jnp.einsum("fv,vh->fh", self_x, slope_one, preferred_element_type=jnp.float32),
            jnp.einsum("fv,vh->fh", aggregate_one, slope_one, preferred_element_type=jnp.float32),
        ]
    )

    one_part = jnp.transpose(
        local_one.reshape(2, feat_devs, cols_dev, hidden_width), (1, 0, 2, 3)
    ).reshape(feat_devs, -1)
    two_part = local_two.reshape(feat_devs, -1)
    outgoing_grad = jnp.concatenate([one_part, two_part], axis=1)
    incoming_grad = lax.all_to_all(outgoing_grad, "feat", split_axis=0, concat_axis=0, tiled=True)
    feat_summed = jnp.sum(incoming_grad, axis=0)
    rep_copies = jnp.broadcast_to(feat_summed[None], (rep_devs,) + feat_summed.shape)
    reduced = jnp.sum(
        lax.all_to_all(rep_copies, "rep", split_axis=0, concat_axis=0, tiled=True), axis=0
    )
    one_size = one_part.shape[1]
    grad_one = reduced[:one_size].reshape(2, cols_dev, hidden_width)
    two_piece = reduced[one_size:]
    two_copies = jnp.broadcast_to(two_piece[None], (feat_devs,) + two_piece.shape)
    grad_two = lax.all_to_all(
        two_copies, "feat", split_axis=0, concat_axis=0, tiled=True
    ).reshape(local_two.shape)
    return (hidden_two[None], grad_one, grad_two)


def solution(mesh):
    return jax.shard_map(
        on_device,
        mesh=mesh,
        in_specs=(
            P("rep", "feat", None),
            P("rep", None, None),
            P(None, "feat", None),
            P(),
            P("rep", "feat", None, None),
            P("rep", "feat", None),
            P("rep", None, "feat"),
            P("rep", "feat", None),
        ),
        out_specs=(P("rep", "feat", None), P(None, "feat", None), P()),
        check_vma=False,
    )
```

```python
import math

import jax
import jax.numpy as jnp
from jax import lax
from jax.sharding import PartitionSpec as P

BLOCK_NODES = 512


def activate(pre):
    return jnp.where(pre > 0.0, pre, jnp.expm1(jnp.minimum(pre, 0.0)))


def elu_slope(pre):
    return jnp.where(pre > 0.0, jnp.ones_like(pre), jnp.exp(jnp.minimum(pre, 0.0)))


def butterfly_reduce_scatter(pieces, steps):
    for axis_name, bit in steps:
        mine = (lax.axis_index(axis_name) >> bit) & 1
        keep = lax.dynamic_index_in_dim(pieces, mine, axis=0, keepdims=False)
        send = lax.dynamic_index_in_dim(pieces, 1 - mine, axis=0, keepdims=False)
        size = lax.axis_size(axis_name)
        pairs = [(i, i ^ (1 << bit)) for i in range(size)]
        pieces = keep + lax.ppermute(send, axis_name, pairs)
    return pieces


def butterfly_all_gather(block, steps):
    for axis_name, bit in reversed(steps):
        mine = (lax.axis_index(axis_name) >> bit) & 1
        size = lax.axis_size(axis_name)
        pairs = [(i, i ^ (1 << bit)) for i in range(size)]
        other = lax.ppermute(block, axis_name, pairs)
        low = jnp.where(mine == 0, block, other)
        high = jnp.where(mine == 0, other, block)
        block = jnp.stack([low, high], axis=0)
    return block


def bit_steps(axis_name, size):
    return [(axis_name, bit) for bit in range(size.bit_length() - 1)]


def on_device(
    features, neighbors_one, weight_one, weight_two, send_rows, halo_count, neighbors_two, cotangent
):
    feat_devs = lax.axis_size("feat")
    rep_devs = lax.axis_size("rep")
    me = lax.axis_index("feat")
    table_x = features[0]
    cols_dev, sources = table_x.shape
    index_one = neighbors_one[0]
    fanout_one, layer_rows = index_one.shape
    node_count = layer_rows // feat_devs
    hidden_width = weight_one.shape[2]
    span_width = 2 * BLOCK_NODES
    span_count = sources // span_width
    nodes_per_span = BLOCK_NODES // node_count

    block_part = jnp.repeat(
        jnp.transpose(table_x.reshape(cols_dev, span_count, span_width), (1, 0, 2)),
        nodes_per_span,
        axis=0,
    )[: feat_devs]
    self_part = jnp.transpose(
        table_x[:, :layer_rows].reshape(cols_dev, feat_devs, node_count), (1, 0, 2)
    )
    weight_part = jnp.transpose(weight_one, (1, 0, 2)).reshape(cols_dev, 2 * hidden_width)
    weight_part = jnp.broadcast_to(weight_part[None], (feat_devs, cols_dev, 2 * hidden_width))
    outgoing_one = jnp.concatenate([block_part, self_part, weight_part], axis=2)
    incoming_one = lax.all_to_all(outgoing_one, "feat", split_axis=0, concat_axis=0, tiled=True)
    gathered = incoming_one.reshape(feat_devs * cols_dev, -1)
    block_x = gathered[:, :span_width]
    self_x = gathered[:, span_width : span_width + node_count]
    full_weight = gathered[:, span_width + node_count :].reshape(-1, 2, hidden_width)

    my_index = lax.dynamic_slice_in_dim(index_one, me * node_count, node_count, axis=1)
    block_start = (me * node_count) // BLOCK_NODES * span_width
    relative = my_index - block_start
    positions = lax.broadcasted_iota(jnp.int32, (node_count, span_width), 1)
    tallies = jnp.zeros((node_count, span_width), jnp.float32)
    for sample in range(fanout_one):
        tallies = tallies + (relative[sample][:, None] == positions).astype(jnp.float32)
    tallies = tallies.astype(jnp.bfloat16)
    summed_one = jnp.einsum("fs,vs->fv", block_x, tallies, preferred_element_type=jnp.float32)
    aggregate_one = (summed_one / fanout_one).astype(jnp.bfloat16)

    pre_one = jnp.einsum(
        "fv,fh->vh", self_x, full_weight[:, 0], preferred_element_type=jnp.float32
    ) + jnp.einsum("fv,fh->vh", aggregate_one, full_weight[:, 1], preferred_element_type=jnp.float32)
    hidden_one = activate(pre_one).astype(jnp.bfloat16)

    send_slots = send_rows[0, 0]
    counts = halo_count[0, 0]
    peers, capacity = send_slots.shape
    live_slots = lax.broadcasted_iota(jnp.int32, send_slots.shape, 1) < counts[:, None]
    local_rows = lax.broadcasted_iota(jnp.int32, (peers, capacity, node_count), 2)
    picks = ((send_slots[:, :, None] == local_rows) & live_slots[:, :, None]).astype(jnp.bfloat16)
    picks = picks.reshape(peers * capacity, node_count)
    outgoing = jnp.einsum(
        "ji,ih->jh", picks, hidden_one, preferred_element_type=jnp.float32
    ).astype(jnp.bfloat16)
    incoming = lax.all_to_all(
        outgoing.reshape(peers, capacity, hidden_width), "feat", split_axis=0, concat_axis=0, tiled=True
    )
    table_two = jnp.concatenate(
        [hidden_one, incoming.reshape(feat_devs * capacity, hidden_width)], axis=0
    )
    index_two = neighbors_two[0]
    fanout_two = index_two.shape[0]
    seed_rows = index_two.shape[1]
    table_rows = table_two.shape[0]
    rows_two = lax.broadcasted_iota(jnp.int32, (seed_rows, table_rows), 1)
    tallies_two = jnp.zeros((seed_rows, table_rows), jnp.float32)
    for sample in range(fanout_two):
        tallies_two = tallies_two + (index_two[sample][:, None] == rows_two).astype(jnp.float32)
    summed_two = jnp.einsum(
        "dr,rh->dh", tallies_two.astype(jnp.bfloat16), table_two, preferred_element_type=jnp.float32
    )
    aggregate_two = (summed_two / fanout_two).astype(jnp.bfloat16)
    pre_two = jnp.dot(hidden_one, weight_two[0], preferred_element_type=jnp.float32) + jnp.dot(
        aggregate_two, weight_two[1], preferred_element_type=jnp.float32
    )
    hidden_two = activate(pre_two).astype(jnp.bfloat16)
    grad_scale = 1.0 / math.sqrt(rep_devs * feat_devs * seed_rows)
    slope_two = (cotangent[0].astype(jnp.float32) * elu_slope(pre_two) * grad_scale).astype(
        jnp.bfloat16
    )
    local_two = jnp.stack(
        [
            jnp.einsum("rh,rk->hk", hidden_one, slope_two, preferred_element_type=jnp.float32),
            jnp.einsum("rh,rk->hk", aggregate_two, slope_two, preferred_element_type=jnp.float32),
        ]
    )
    all_steps = bit_steps("feat", feat_devs) + bit_steps("rep", rep_devs)
    two_shape = (2,) * len(all_steps) + (-1,)
    two_block = butterfly_reduce_scatter(local_two.reshape(two_shape), all_steps)
    grad_two = butterfly_all_gather(two_block, all_steps).reshape(local_two.shape)
    back_self = jnp.einsum(
        "rk,hk->rh", slope_two, weight_two[0], preferred_element_type=jnp.float32
    )
    back_agg = (
        jnp.einsum("rk,hk->rh", slope_two, weight_two[1], preferred_element_type=jnp.float32)
        / fanout_two
    )
    grad_table = jnp.einsum(
        "dr,dh->rh", tallies_two, back_agg, precision=lax.Precision.HIGHEST,
        preferred_element_type=jnp.float32,
    )
    returned = lax.all_to_all(
        grad_table[node_count:].reshape(peers, capacity, hidden_width).astype(jnp.bfloat16),
        "feat",
        split_axis=0,
        concat_axis=0,
        tiled=True,
    )
    back_one = grad_table[:node_count] + back_self + jnp.einsum(
        "ji,jh->ih", picks, returned.reshape(peers * capacity, hidden_width),
        preferred_element_type=jnp.float32,
    )
    slope_one = (back_one * elu_slope(pre_one)).astype(jnp.bfloat16)
    local_one = jnp.stack(
        [
            jnp.einsum("fv,vh->fh", self_x, slope_one, preferred_element_type=jnp.float32),
            jnp.einsum("fv,vh->fh", aggregate_one, slope_one, preferred_element_type=jnp.float32),
        ]
    )

    feat_steps = bit_steps("feat", feat_devs)
    bits = len(feat_steps)
    one_split = local_one.reshape((2,) + (2,) * bits + (cols_dev, hidden_width))
    order = tuple(range(bits, 0, -1)) + (0, bits + 1, bits + 2)
    one_block = butterfly_reduce_scatter(jnp.transpose(one_split, order), feat_steps)
    for axis_name, bit in bit_steps("rep", rep_devs):
        pairs = [(i, i ^ (1 << bit)) for i in range(rep_devs)]
        one_block = one_block + lax.ppermute(one_block, axis_name, pairs)
    grad_one = one_block
    return (hidden_two[None], grad_one, grad_two)


def solution(mesh):
    return jax.shard_map(
        on_device,
        mesh=mesh,
        in_specs=(
            P("rep", "feat", None),
            P("rep", None, None),
            P(None, "feat", None),
            P(),
            P("rep", "feat", None, None),
            P("rep", "feat", None),
            P("rep", None, "feat"),
            P("rep", "feat", None),
        ),
        out_specs=(P("rep", "feat", None), P(None, "feat", None), P()),
        check_vma=False,
    )
```

```python
import math

import jax
import jax.numpy as jnp
from jax import lax
from jax.sharding import PartitionSpec as P

BLOCK_NODES = 512


def activate(pre):
    return jnp.where(pre > 0.0, pre, jnp.expm1(jnp.minimum(pre, 0.0)))


def elu_slope(pre):
    return jnp.where(pre > 0.0, jnp.ones_like(pre), jnp.exp(jnp.minimum(pre, 0.0)))


def group_pairs(axis_name, stride, group, shift):
    size = lax.axis_size(axis_name)
    pairs = []
    for i in range(size):
        place = (i // stride) % group
        pairs.append((i, i + ((place + shift) % group - place) * stride))
    return pairs


def group_place(axis_name, stride, group):
    return (lax.axis_index(axis_name) // stride) % group


def group_reduce_scatter(pieces, steps):
    for axis_name, stride, group in steps:
        rolled = jnp.roll(pieces, -group_place(axis_name, stride, group), axis=0)
        total = rolled[0]
        for shift in range(1, group):
            total = total + lax.ppermute(
                rolled[shift], axis_name, group_pairs(axis_name, stride, group, shift)
            )
        pieces = total
    return pieces


def group_all_gather(block, steps):
    for axis_name, stride, group in reversed(steps):
        parts = [block]
        for shift in range(group - 1, 0, -1):
            parts.append(
                lax.ppermute(block, axis_name, group_pairs(axis_name, stride, group, shift))
            )
        block = jnp.roll(jnp.stack(parts), group_place(axis_name, stride, group), axis=0)
    return block


def torus_steps(mesh_axes):
    steps = []
    for axis_name, sizes in mesh_axes:
        stride = 1
        for group in reversed(sizes):
            steps.append((axis_name, stride, group))
            stride *= group
    return steps


def on_device(
    features, neighbors_one, weight_one, weight_two, send_rows, halo_count, neighbors_two, cotangent
):
    feat_devs = lax.axis_size("feat")
    rep_devs = lax.axis_size("rep")
    me = lax.axis_index("feat")
    table_x = features[0]
    cols_dev, sources = table_x.shape
    index_one = neighbors_one[0]
    fanout_one, layer_rows = index_one.shape
    node_count = layer_rows // feat_devs
    hidden_width = weight_one.shape[2]
    span_width = 2 * BLOCK_NODES
    span_count = sources // span_width
    nodes_per_span = BLOCK_NODES // node_count

    block_part = jnp.repeat(
        jnp.transpose(table_x.reshape(cols_dev, span_count, span_width), (1, 0, 2)),
        nodes_per_span,
        axis=0,
    )[: feat_devs]
    self_part = jnp.transpose(
        table_x[:, :layer_rows].reshape(cols_dev, feat_devs, node_count), (1, 0, 2)
    )
    weight_part = jnp.transpose(weight_one, (1, 0, 2)).reshape(cols_dev, 2 * hidden_width)
    weight_part = jnp.broadcast_to(weight_part[None], (feat_devs, cols_dev, 2 * hidden_width))
    outgoing_one = jnp.concatenate([block_part, self_part, weight_part], axis=2)
    incoming_one = lax.all_to_all(outgoing_one, "feat", split_axis=0, concat_axis=0, tiled=True)
    gathered = incoming_one.reshape(feat_devs * cols_dev, -1)
    block_x = gathered[:, :span_width]
    self_x = gathered[:, span_width : span_width + node_count]
    full_weight = gathered[:, span_width + node_count :].reshape(-1, 2, hidden_width)

    my_index = lax.dynamic_slice_in_dim(index_one, me * node_count, node_count, axis=1)
    block_start = (me * node_count) // BLOCK_NODES * span_width
    relative = my_index - block_start
    positions = lax.broadcasted_iota(jnp.int32, (node_count, span_width), 1)
    tallies = jnp.zeros((node_count, span_width), jnp.float32)
    for sample in range(fanout_one):
        tallies = tallies + (relative[sample][:, None] == positions).astype(jnp.float32)
    tallies = tallies.astype(jnp.bfloat16)
    summed_one = jnp.einsum("fs,vs->fv", block_x, tallies, preferred_element_type=jnp.float32)
    aggregate_one = (summed_one / fanout_one).astype(jnp.bfloat16)

    pre_one = jnp.einsum(
        "fv,fh->vh", self_x, full_weight[:, 0], preferred_element_type=jnp.float32
    ) + jnp.einsum("fv,fh->vh", aggregate_one, full_weight[:, 1], preferred_element_type=jnp.float32)
    hidden_one = activate(pre_one).astype(jnp.bfloat16)

    send_slots = send_rows[0, 0]
    counts = halo_count[0, 0]
    peers, capacity = send_slots.shape
    live_slots = lax.broadcasted_iota(jnp.int32, send_slots.shape, 1) < counts[:, None]
    local_rows = lax.broadcasted_iota(jnp.int32, (peers, capacity, node_count), 2)
    picks = ((send_slots[:, :, None] == local_rows) & live_slots[:, :, None]).astype(jnp.bfloat16)
    picks = picks.reshape(peers * capacity, node_count)
    outgoing = jnp.einsum(
        "ji,ih->jh", picks, hidden_one, preferred_element_type=jnp.float32
    ).astype(jnp.bfloat16)
    incoming = lax.all_to_all(
        outgoing.reshape(peers, capacity, hidden_width), "feat", split_axis=0, concat_axis=0, tiled=True
    )
    table_two = jnp.concatenate(
        [hidden_one, incoming.reshape(feat_devs * capacity, hidden_width)], axis=0
    )
    index_two = neighbors_two[0]
    fanout_two = index_two.shape[0]
    seed_rows = index_two.shape[1]
    table_rows = table_two.shape[0]
    rows_two = lax.broadcasted_iota(jnp.int32, (seed_rows, table_rows), 1)
    tallies_two = jnp.zeros((seed_rows, table_rows), jnp.float32)
    for sample in range(fanout_two):
        tallies_two = tallies_two + (index_two[sample][:, None] == rows_two).astype(jnp.float32)
    summed_two = jnp.einsum(
        "dr,rh->dh", tallies_two.astype(jnp.bfloat16), table_two, preferred_element_type=jnp.float32
    )
    aggregate_two = (summed_two / fanout_two).astype(jnp.bfloat16)
    pre_two = jnp.dot(hidden_one, weight_two[0], preferred_element_type=jnp.float32) + jnp.dot(
        aggregate_two, weight_two[1], preferred_element_type=jnp.float32
    )
    hidden_two = activate(pre_two).astype(jnp.bfloat16)
    grad_scale = 1.0 / math.sqrt(rep_devs * feat_devs * seed_rows)
    slope_two = (cotangent[0].astype(jnp.float32) * elu_slope(pre_two) * grad_scale).astype(
        jnp.bfloat16
    )
    local_two = jnp.stack(
        [
            jnp.einsum("rh,rk->hk", hidden_one, slope_two, preferred_element_type=jnp.float32),
            jnp.einsum("rh,rk->hk", aggregate_two, slope_two, preferred_element_type=jnp.float32),
        ]
    )
    feat_parts = (feat_devs // 16, 8, 2)
    feat_steps = torus_steps([("feat", feat_parts)])
    all_steps = feat_steps + torus_steps([("rep", (rep_devs,))])
    two_shape = tuple(group for _, _, group in all_steps) + (-1,)
    two_block = group_reduce_scatter(local_two.reshape(two_shape), all_steps)
    grad_two = group_all_gather(two_block, all_steps).reshape(local_two.shape)
    back_self = jnp.einsum(
        "rk,hk->rh", slope_two, weight_two[0], preferred_element_type=jnp.float32
    )
    back_agg = (
        jnp.einsum("rk,hk->rh", slope_two, weight_two[1], preferred_element_type=jnp.float32)
        / fanout_two
    )
    agg_high = back_agg.astype(jnp.bfloat16)
    agg_low = (back_agg - agg_high.astype(jnp.float32)).astype(jnp.bfloat16)
    tallies_bf = tallies_two.astype(jnp.bfloat16)
    grad_table = jnp.einsum(
        "dr,dh->rh", tallies_bf, agg_high, preferred_element_type=jnp.float32
    ) + jnp.einsum("dr,dh->rh", tallies_bf, agg_low, preferred_element_type=jnp.float32)
    returned = lax.all_to_all(
        grad_table[node_count:].reshape(peers, capacity, hidden_width).astype(jnp.bfloat16),
        "feat",
        split_axis=0,
        concat_axis=0,
        tiled=True,
    )
    back_one = grad_table[:node_count] + back_self + jnp.einsum(
        "ji,jh->ih", picks, returned.reshape(peers * capacity, hidden_width),
        preferred_element_type=jnp.float32,
    )
    slope_one = (back_one * elu_slope(pre_one)).astype(jnp.bfloat16)
    local_one = jnp.stack(
        [
            jnp.einsum("fv,vh->fh", self_x, slope_one, preferred_element_type=jnp.float32),
            jnp.einsum("fv,vh->fh", aggregate_one, slope_one, preferred_element_type=jnp.float32),
        ]
    )

    one_split = local_one.reshape((2,) + feat_parts + (cols_dev, hidden_width))
    one_block = group_reduce_scatter(jnp.transpose(one_split, (3, 2, 1, 0, 4, 5)), feat_steps)
    grad_one = one_block
    for shift in range(1, rep_devs):
        grad_one = grad_one + lax.ppermute(one_block, "rep", group_pairs("rep", 1, rep_devs, shift))
    return (hidden_two[None], grad_one, grad_two)


def solution(mesh):
    return jax.shard_map(
        on_device,
        mesh=mesh,
        in_specs=(
            P("rep", "feat", None),
            P("rep", None, None),
            P(None, "feat", None),
            P(),
            P("rep", "feat", None, None),
            P("rep", "feat", None),
            P("rep", None, "feat"),
            P("rep", "feat", None),
        ),
        out_specs=(P("rep", "feat", None), P(None, "feat", None), P()),
        check_vma=False,
    )
```

```python
import math

import jax
import jax.numpy as jnp
from jax import lax
from jax.sharding import PartitionSpec as P

BLOCK_NODES = 512


def activate(pre):
    return jnp.where(pre > 0.0, pre, jnp.expm1(jnp.minimum(pre, 0.0)))


def elu_slope(pre):
    return jnp.where(pre > 0.0, jnp.ones_like(pre), jnp.exp(jnp.minimum(pre, 0.0)))


def on_device(
    features, neighbors_one, weight_one, weight_two, send_rows, halo_count, neighbors_two, cotangent
):
    feat_devs = lax.axis_size("feat")
    rep_devs = lax.axis_size("rep")
    me = lax.axis_index("feat")
    table_x = features[0]
    cols_dev, sources = table_x.shape
    index_one = neighbors_one[0]
    fanout_one, layer_rows = index_one.shape
    node_count = layer_rows // feat_devs
    hidden_width = weight_one.shape[2]
    span_width = 2 * BLOCK_NODES
    span_count = sources // span_width
    nodes_per_span = BLOCK_NODES // node_count

    block_part = jnp.repeat(
        jnp.transpose(table_x.reshape(cols_dev, span_count, span_width), (1, 0, 2)),
        nodes_per_span,
        axis=0,
    )[: feat_devs]
    self_part = jnp.transpose(
        table_x[:, :layer_rows].reshape(cols_dev, feat_devs, node_count), (1, 0, 2)
    )
    weight_part = jnp.transpose(weight_one, (1, 0, 2)).reshape(cols_dev, 2 * hidden_width)
    weight_part = jnp.broadcast_to(weight_part[None], (feat_devs, cols_dev, 2 * hidden_width))
    outgoing_one = jnp.concatenate([block_part, self_part, weight_part], axis=2)
    lanes = 128
    outgoing_one = outgoing_one.reshape(feat_devs, -1, lanes)
    incoming_one = lax.all_to_all(outgoing_one, "feat", split_axis=0, concat_axis=0, tiled=True)
    gathered = incoming_one.reshape(feat_devs * cols_dev, -1)
    block_x = gathered[:, :span_width]
    self_x = gathered[:, span_width : span_width + node_count]
    full_weight = gathered[:, span_width + node_count :].reshape(-1, 2, hidden_width)

    my_index = lax.dynamic_slice_in_dim(index_one, me * node_count, node_count, axis=1)
    block_start = (me * node_count) // BLOCK_NODES * span_width
    relative = my_index - block_start
    positions = lax.broadcasted_iota(jnp.int32, (node_count, span_width), 1)
    tallies = jnp.zeros((node_count, span_width), jnp.float32)
    for sample in range(fanout_one):
        tallies = tallies + (relative[sample][:, None] == positions).astype(jnp.float32)
    tallies = tallies.astype(jnp.bfloat16)
    summed_one = jnp.einsum("fs,vs->fv", block_x, tallies, preferred_element_type=jnp.float32)
    aggregate_one = (summed_one / fanout_one).astype(jnp.bfloat16)

    pre_one = jnp.einsum(
        "fv,fh->vh", self_x, full_weight[:, 0], preferred_element_type=jnp.float32
    ) + jnp.einsum("fv,fh->vh", aggregate_one, full_weight[:, 1], preferred_element_type=jnp.float32)
    hidden_one = activate(pre_one).astype(jnp.bfloat16)

    send_slots = send_rows[0, 0]
    counts = halo_count[0, 0]
    peers, capacity = send_slots.shape
    live_slots = lax.broadcasted_iota(jnp.int32, send_slots.shape, 1) < counts[:, None]
    local_rows = lax.broadcasted_iota(jnp.int32, (peers, capacity, node_count), 2)
    picks = ((send_slots[:, :, None] == local_rows) & live_slots[:, :, None]).astype(jnp.bfloat16)
    picks = picks.reshape(peers * capacity, node_count)
    outgoing = jnp.einsum(
        "ji,ih->jh", picks, hidden_one, preferred_element_type=jnp.float32
    ).astype(jnp.bfloat16)
    incoming = lax.all_to_all(
        outgoing.reshape(peers, capacity, hidden_width), "feat", split_axis=0, concat_axis=0, tiled=True
    )
    table_two = jnp.concatenate(
        [hidden_one, incoming.reshape(feat_devs * capacity, hidden_width)], axis=0
    )
    index_two = neighbors_two[0]
    fanout_two = index_two.shape[0]
    seed_rows = index_two.shape[1]
    table_rows = table_two.shape[0]
    rows_two = lax.broadcasted_iota(jnp.int32, (seed_rows, table_rows), 1)
    tallies_two = jnp.zeros((seed_rows, table_rows), jnp.float32)
    for sample in range(fanout_two):
        tallies_two = tallies_two + (index_two[sample][:, None] == rows_two).astype(jnp.float32)
    summed_two = jnp.einsum(
        "dr,rh->dh", tallies_two.astype(jnp.bfloat16), table_two, preferred_element_type=jnp.float32
    )
    aggregate_two = (summed_two / fanout_two).astype(jnp.bfloat16)
    pre_two = jnp.dot(hidden_one, weight_two[0], preferred_element_type=jnp.float32) + jnp.dot(
        aggregate_two, weight_two[1], preferred_element_type=jnp.float32
    )
    hidden_two = activate(pre_two).astype(jnp.bfloat16)
    grad_scale = 1.0 / math.sqrt(rep_devs * feat_devs * seed_rows)
    slope_two = (cotangent[0].astype(jnp.float32) * elu_slope(pre_two) * grad_scale).astype(
        jnp.bfloat16
    )
    local_two = jnp.stack(
        [
            jnp.einsum("rh,rk->hk", hidden_one, slope_two, preferred_element_type=jnp.float32),
            jnp.einsum("rh,rk->hk", aggregate_two, slope_two, preferred_element_type=jnp.float32),
        ]
    )
    back_self = jnp.einsum(
        "rk,hk->rh", slope_two, weight_two[0], preferred_element_type=jnp.float32
    )
    back_agg = (
        jnp.einsum("rk,hk->rh", slope_two, weight_two[1], preferred_element_type=jnp.float32)
        / fanout_two
    )
    agg_high = back_agg.astype(jnp.bfloat16)
    agg_low = (back_agg - agg_high.astype(jnp.float32)).astype(jnp.bfloat16)
    tallies_bf = tallies_two.astype(jnp.bfloat16)
    grad_table = jnp.einsum(
        "dr,dh->rh", tallies_bf, agg_high, preferred_element_type=jnp.float32
    ) + jnp.einsum("dr,dh->rh", tallies_bf, agg_low, preferred_element_type=jnp.float32)
    returned = lax.all_to_all(
        grad_table[node_count:].reshape(peers, capacity, hidden_width).astype(jnp.bfloat16),
        "feat",
        split_axis=0,
        concat_axis=0,
        tiled=True,
    )
    back_one = grad_table[:node_count] + back_self + jnp.einsum(
        "ji,jh->ih", picks, returned.reshape(peers * capacity, hidden_width),
        preferred_element_type=jnp.float32,
    )
    slope_one = (back_one * elu_slope(pre_one)).astype(jnp.bfloat16)
    local_one = jnp.stack(
        [
            jnp.einsum("fv,vh->fh", self_x, slope_one, preferred_element_type=jnp.float32),
            jnp.einsum("fv,vh->fh", aggregate_one, slope_one, preferred_element_type=jnp.float32),
        ]
    )

    one_part = jnp.transpose(
        local_one.reshape(2, feat_devs, cols_dev, hidden_width), (1, 0, 2, 3)
    ).reshape(feat_devs, -1)
    two_part = local_two.reshape(feat_devs, -1)
    outgoing_grad = jnp.concatenate([one_part, two_part], axis=1)
    incoming_grad = lax.all_to_all(outgoing_grad, "feat", split_axis=0, concat_axis=0, tiled=True)
    feat_summed = jnp.sum(incoming_grad, axis=0)
    reduced = feat_summed
    for bit in range(rep_devs.bit_length() - 1):
        pairs = [(i, i ^ (1 << bit)) for i in range(rep_devs)]
        reduced = reduced + lax.ppermute(reduced, "rep", pairs)
    one_size = one_part.shape[1]
    grad_one = reduced[:one_size].reshape(2, cols_dev, hidden_width)
    two_piece = reduced[one_size:]
    two_copies = jnp.broadcast_to(two_piece[None], (feat_devs,) + two_piece.shape)
    grad_two = lax.all_to_all(
        two_copies, "feat", split_axis=0, concat_axis=0, tiled=True
    ).reshape(local_two.shape)
    return (hidden_two[None], grad_one, grad_two)


def solution(mesh):
    return jax.shard_map(
        on_device,
        mesh=mesh,
        in_specs=(
            P("rep", "feat", None),
            P("rep", None, None),
            P(None, "feat", None),
            P(),
            P("rep", "feat", None, None),
            P("rep", "feat", None),
            P("rep", None, "feat"),
            P("rep", "feat", None),
        ),
        out_specs=(P("rep", "feat", None), P(None, "feat", None), P()),
        check_vma=False,
    )
```

```python
import math

import jax
import jax.numpy as jnp
from jax import lax
from jax.sharding import PartitionSpec as P

BLOCK_NODES = 512


def activate(pre):
    return jnp.where(pre > 0.0, pre, jnp.expm1(jnp.minimum(pre, 0.0)))


def elu_slope(pre):
    return jnp.where(pre > 0.0, jnp.ones_like(pre), jnp.exp(jnp.minimum(pre, 0.0)))


def on_device(
    features, neighbors_one, weight_one, weight_two, send_rows, halo_count, neighbors_two, cotangent
):
    feat_devs = lax.axis_size("feat")
    rep_devs = lax.axis_size("rep")
    me = lax.axis_index("feat")
    table_x = features[0]
    cols_dev, sources = table_x.shape
    index_one = neighbors_one[0]
    fanout_one, layer_rows = index_one.shape
    node_count = layer_rows // feat_devs
    hidden_width = weight_one.shape[2]
    span_width = 2 * BLOCK_NODES
    span_count = sources // span_width
    nodes_per_span = BLOCK_NODES // node_count

    block_part = jnp.repeat(
        jnp.transpose(table_x.reshape(cols_dev, span_count, span_width), (1, 0, 2)),
        nodes_per_span,
        axis=0,
    )[: feat_devs]
    self_part = jnp.transpose(
        table_x[:, :layer_rows].reshape(cols_dev, feat_devs, node_count), (1, 0, 2)
    )
    weight_part = jnp.transpose(weight_one, (1, 0, 2)).reshape(cols_dev, 2 * hidden_width)
    weight_part = jnp.broadcast_to(weight_part[None], (feat_devs, cols_dev, 2 * hidden_width))
    outgoing_one = jnp.concatenate([block_part, self_part, weight_part], axis=2)
    incoming_one = lax.all_to_all(outgoing_one, "feat", split_axis=0, concat_axis=0, tiled=True)
    gathered = incoming_one.reshape(feat_devs * cols_dev, -1)
    block_x = gathered[:, :span_width]
    self_x = gathered[:, span_width : span_width + node_count]
    full_weight = gathered[:, span_width + node_count :].reshape(-1, 2, hidden_width)

    my_index = lax.dynamic_slice_in_dim(index_one, me * node_count, node_count, axis=1)
    block_start = (me * node_count) // BLOCK_NODES * span_width
    relative = my_index - block_start
    positions = lax.broadcasted_iota(jnp.int32, (node_count, span_width), 1)
    tallies = jnp.zeros((node_count, span_width), jnp.float32)
    for sample in range(fanout_one):
        tallies = tallies + (relative[sample][:, None] == positions).astype(jnp.float32)
    tallies = tallies.astype(jnp.bfloat16)
    summed_one = jnp.einsum("fs,vs->fv", block_x, tallies, preferred_element_type=jnp.float32)
    aggregate_one = (summed_one / fanout_one).astype(jnp.bfloat16)

    pre_one = jnp.einsum(
        "fv,fh->vh", self_x, full_weight[:, 0], preferred_element_type=jnp.float32
    ) + jnp.einsum("fv,fh->vh", aggregate_one, full_weight[:, 1], preferred_element_type=jnp.float32)
    hidden_one = activate(pre_one).astype(jnp.bfloat16)

    send_slots = send_rows[0, 0]
    counts = halo_count[0, 0]
    peers, capacity = send_slots.shape
    live_slots = lax.broadcasted_iota(jnp.int32, send_slots.shape, 1) < counts[:, None]
    local_rows = lax.broadcasted_iota(jnp.int32, (peers, capacity, node_count), 2)
    picks = ((send_slots[:, :, None] == local_rows) & live_slots[:, :, None]).astype(jnp.bfloat16)
    picks = picks.reshape(peers * capacity, node_count)
    outgoing = jnp.einsum(
        "ji,ih->jh", picks, hidden_one, preferred_element_type=jnp.float32
    ).astype(jnp.bfloat16)
    incoming = lax.all_to_all(
        outgoing.reshape(peers, capacity, hidden_width), "feat", split_axis=0, concat_axis=0, tiled=True
    )
    table_two = jnp.concatenate(
        [hidden_one, incoming.reshape(feat_devs * capacity, hidden_width)], axis=0
    )
    index_two = neighbors_two[0]
    fanout_two = index_two.shape[0]
    seed_rows = index_two.shape[1]
    table_rows = table_two.shape[0]
    rows_two = lax.broadcasted_iota(jnp.int32, (seed_rows, table_rows), 1)
    tallies_two = jnp.zeros((seed_rows, table_rows), jnp.float32)
    for sample in range(fanout_two):
        tallies_two = tallies_two + (index_two[sample][:, None] == rows_two).astype(jnp.float32)
    summed_two = jnp.einsum(
        "dr,rh->dh", tallies_two.astype(jnp.bfloat16), table_two, preferred_element_type=jnp.float32
    )
    aggregate_two = (summed_two / fanout_two).astype(jnp.bfloat16)
    pre_two = jnp.dot(hidden_one, weight_two[0], preferred_element_type=jnp.float32) + jnp.dot(
        aggregate_two, weight_two[1], preferred_element_type=jnp.float32
    )
    hidden_two = activate(pre_two).astype(jnp.bfloat16)
    grad_scale = 1.0 / math.sqrt(rep_devs * feat_devs * seed_rows)
    slope_two = (cotangent[0].astype(jnp.float32) * elu_slope(pre_two) * grad_scale).astype(
        jnp.bfloat16
    )
    local_two = jnp.stack(
        [
            jnp.einsum("rh,rk->hk", hidden_one, slope_two, preferred_element_type=jnp.float32),
            jnp.einsum("rh,rk->hk", aggregate_two, slope_two, preferred_element_type=jnp.float32),
        ]
    )
    back_self = jnp.einsum(
        "rk,hk->rh", slope_two, weight_two[0], preferred_element_type=jnp.float32
    )
    back_agg = (
        jnp.einsum("rk,hk->rh", slope_two, weight_two[1], preferred_element_type=jnp.float32)
        / fanout_two
    )
    grad_table = jnp.einsum(
        "dr,dh->rh", tallies_two, back_agg, precision=lax.Precision.HIGHEST,
        preferred_element_type=jnp.float32,
    )
    returned = lax.all_to_all(
        grad_table[node_count:].reshape(peers, capacity, hidden_width).astype(jnp.bfloat16),
        "feat",
        split_axis=0,
        concat_axis=0,
        tiled=True,
    )
    back_one = grad_table[:node_count] + back_self + jnp.einsum(
        "ji,jh->ih", picks, returned.reshape(peers * capacity, hidden_width),
        preferred_element_type=jnp.float32,
    )
    slope_one = (back_one * elu_slope(pre_one)).astype(jnp.bfloat16)
    local_one = jnp.stack(
        [
            jnp.einsum("fv,vh->fh", self_x, slope_one, preferred_element_type=jnp.float32),
            jnp.einsum("fv,vh->fh", aggregate_one, slope_one, preferred_element_type=jnp.float32),
        ]
    )

    one_part = jnp.transpose(
        local_one.reshape(2, feat_devs, cols_dev, hidden_width), (1, 0, 2, 3)
    ).reshape(feat_devs, -1)
    two_part = local_two.reshape(feat_devs, -1)
    outgoing_grad = jnp.concatenate([one_part, two_part], axis=1)
    incoming_grad = lax.all_to_all(outgoing_grad, "feat", split_axis=0, concat_axis=0, tiled=True)
    feat_summed = jnp.sum(incoming_grad, axis=0)
    rep_copies = jnp.broadcast_to(feat_summed[None], (rep_devs,) + feat_summed.shape)
    reduced = jnp.sum(
        lax.all_to_all(rep_copies, "rep", split_axis=0, concat_axis=0, tiled=True), axis=0
    )
    one_size = one_part.shape[1]
    grad_one = reduced[:one_size].reshape(2, cols_dev, hidden_width)
    two_piece = reduced[one_size:].astype(jnp.bfloat16)
    two_copies = jnp.broadcast_to(two_piece[None], (feat_devs,) + two_piece.shape)
    grad_two = lax.all_to_all(
        two_copies, "feat", split_axis=0, concat_axis=0, tiled=True
    ).astype(jnp.float32).reshape(local_two.shape)
    return (hidden_two[None], grad_one, grad_two)


def solution(mesh):
    return jax.shard_map(
        on_device,
        mesh=mesh,
        in_specs=(
            P("rep", "feat", None),
            P("rep", None, None),
            P(None, "feat", None),
            P(),
            P("rep", "feat", None, None),
            P("rep", "feat", None),
            P("rep", None, "feat"),
            P("rep", "feat", None),
        ),
        out_specs=(P("rep", "feat", None), P(None, "feat", None), P()),
        check_vma=False,
    )
```

```python
import math

import jax
import jax.numpy as jnp
from jax import lax
from jax.sharding import PartitionSpec as P

BLOCK_NODES = 512


def activate(pre):
    return jnp.where(pre > 0.0, pre, jnp.expm1(jnp.minimum(pre, 0.0)))


def elu_slope(pre):
    return jnp.where(pre > 0.0, jnp.ones_like(pre), jnp.exp(jnp.minimum(pre, 0.0)))


def on_device(
    features, neighbors_one, weight_one, weight_two, send_rows, halo_count, neighbors_two, cotangent
):
    feat_devs = lax.axis_size("feat")
    rep_devs = lax.axis_size("rep")
    me = lax.axis_index("feat")
    table_x = features[0]
    cols_dev, sources = table_x.shape
    index_one = neighbors_one[0]
    fanout_one, layer_rows = index_one.shape
    node_count = layer_rows // feat_devs
    hidden_width = weight_one.shape[2]
    span_width = 2 * BLOCK_NODES
    span_count = sources // span_width
    nodes_per_span = BLOCK_NODES // node_count

    my_index = lax.dynamic_slice_in_dim(index_one, me * node_count, node_count, axis=1)
    block_start = (me * node_count) // BLOCK_NODES * span_width
    relative = my_index - block_start
    positions = lax.broadcasted_iota(jnp.int32, (node_count, span_width), 1)
    tallies = jnp.zeros((node_count, span_width), jnp.float32)
    for sample in range(fanout_one):
        tallies = tallies + (relative[sample][:, None] == positions).astype(jnp.float32)
    tallies = tallies.astype(jnp.bfloat16)
    send_slots = send_rows[0, 0]
    counts = halo_count[0, 0]
    peers, capacity = send_slots.shape
    live_slots = lax.broadcasted_iota(jnp.int32, send_slots.shape, 1) < counts[:, None]
    local_rows = lax.broadcasted_iota(jnp.int32, (peers, capacity, node_count), 2)
    picks = ((send_slots[:, :, None] == local_rows) & live_slots[:, :, None]).astype(jnp.bfloat16)
    picks = picks.reshape(peers * capacity, node_count)
    index_two = neighbors_two[0]
    fanout_two = index_two.shape[0]
    seed_rows = index_two.shape[1]
    table_rows = node_count + peers * capacity
    rows_two = lax.broadcasted_iota(jnp.int32, (seed_rows, table_rows), 1)
    tallies_two = jnp.zeros((seed_rows, table_rows), jnp.float32)
    for sample in range(fanout_two):
        tallies_two = tallies_two + (index_two[sample][:, None] == rows_two).astype(jnp.float32)
    tallies_two = tallies_two.astype(jnp.bfloat16)
    tallies, picks, tallies_two = lax.optimization_barrier((tallies, picks, tallies_two))

    block_part = jnp.repeat(
        jnp.transpose(table_x.reshape(cols_dev, span_count, span_width), (1, 0, 2)),
        nodes_per_span,
        axis=0,
    )[: feat_devs]
    self_part = jnp.transpose(
        table_x[:, :layer_rows].reshape(cols_dev, feat_devs, node_count), (1, 0, 2)
    )
    weight_part = jnp.transpose(weight_one, (1, 0, 2)).reshape(cols_dev, 2 * hidden_width)
    weight_part = jnp.broadcast_to(weight_part[None], (feat_devs, cols_dev, 2 * hidden_width))
    outgoing_one = jnp.concatenate([block_part, self_part, weight_part], axis=2)
    incoming_one = lax.all_to_all(outgoing_one, "feat", split_axis=0, concat_axis=0, tiled=True)
    gathered = incoming_one.reshape(feat_devs * cols_dev, -1)
    block_x = gathered[:, :span_width]
    self_x = gathered[:, span_width : span_width + node_count]
    full_weight = gathered[:, span_width + node_count :].reshape(-1, 2, hidden_width)

    summed_one = jnp.einsum("fs,vs->fv", block_x, tallies, preferred_element_type=jnp.float32)
    aggregate_one = (summed_one / fanout_one).astype(jnp.bfloat16)

    pre_one = jnp.einsum(
        "fv,fh->vh", self_x, full_weight[:, 0], preferred_element_type=jnp.float32
    ) + jnp.einsum("fv,fh->vh", aggregate_one, full_weight[:, 1], preferred_element_type=jnp.float32)
    hidden_one = activate(pre_one).astype(jnp.bfloat16)

    outgoing = jnp.einsum(
        "ji,ih->jh", picks, hidden_one, preferred_element_type=jnp.float32
    ).astype(jnp.bfloat16)
    incoming = lax.all_to_all(
        outgoing.reshape(peers, capacity, hidden_width), "feat", split_axis=0, concat_axis=0, tiled=True
    )
    table_two = jnp.concatenate(
        [hidden_one, incoming.reshape(feat_devs * capacity, hidden_width)], axis=0
    )
    summed_two = jnp.einsum(
        "dr,rh->dh", tallies_two, table_two, preferred_element_type=jnp.float32
    )
    aggregate_two = (summed_two / fanout_two).astype(jnp.bfloat16)
    pre_two = jnp.dot(hidden_one, weight_two[0], preferred_element_type=jnp.float32) + jnp.dot(
        aggregate_two, weight_two[1], preferred_element_type=jnp.float32
    )
    hidden_two = activate(pre_two).astype(jnp.bfloat16)
    grad_scale = 1.0 / math.sqrt(rep_devs * feat_devs * seed_rows)
    slope_two = (cotangent[0].astype(jnp.float32) * elu_slope(pre_two) * grad_scale).astype(
        jnp.bfloat16
    )
    local_two = jnp.stack(
        [
            jnp.einsum("rh,rk->hk", hidden_one, slope_two, preferred_element_type=jnp.float32),
            jnp.einsum("rh,rk->hk", aggregate_two, slope_two, preferred_element_type=jnp.float32),
        ]
    )
    back_self = jnp.einsum(
        "rk,hk->rh", slope_two, weight_two[0], preferred_element_type=jnp.float32
    )
    back_agg = (
        jnp.einsum("rk,hk->rh", slope_two, weight_two[1], preferred_element_type=jnp.float32)
        / fanout_two
    )
    grad_table = jnp.einsum(
        "dr,dh->rh", tallies_two.astype(jnp.float32), back_agg, precision=lax.Precision.HIGHEST,
        preferred_element_type=jnp.float32,
    )
    returned = lax.all_to_all(
        grad_table[node_count:].reshape(peers, capacity, hidden_width).astype(jnp.bfloat16),
        "feat",
        split_axis=0,
        concat_axis=0,
        tiled=True,
    )
    back_one = grad_table[:node_count] + back_self + jnp.einsum(
        "ji,jh->ih", picks, returned.reshape(peers * capacity, hidden_width),
        preferred_element_type=jnp.float32,
    )
    slope_one = (back_one * elu_slope(pre_one)).astype(jnp.bfloat16)
    local_one = jnp.stack(
        [
            jnp.einsum("fv,vh->fh", self_x, slope_one, preferred_element_type=jnp.float32),
            jnp.einsum("fv,vh->fh", aggregate_one, slope_one, preferred_element_type=jnp.float32),
        ]
    )

    one_part = jnp.transpose(
        local_one.reshape(2, feat_devs, cols_dev, hidden_width), (1, 0, 2, 3)
    ).reshape(feat_devs, -1)
    two_part = local_two.reshape(feat_devs, -1)
    outgoing_grad = jnp.concatenate([one_part, two_part], axis=1)
    incoming_grad = lax.all_to_all(outgoing_grad, "feat", split_axis=0, concat_axis=0, tiled=True)
    feat_summed = jnp.sum(incoming_grad, axis=0)
    rep_copies = jnp.broadcast_to(feat_summed[None], (rep_devs,) + feat_summed.shape)
    reduced = jnp.sum(
        lax.all_to_all(rep_copies, "rep", split_axis=0, concat_axis=0, tiled=True), axis=0
    )
    one_size = one_part.shape[1]
    grad_one = reduced[:one_size].reshape(2, cols_dev, hidden_width)
    two_piece = reduced[one_size:].astype(jnp.bfloat16)
    two_copies = jnp.broadcast_to(two_piece[None], (feat_devs,) + two_piece.shape)
    grad_two = lax.all_to_all(
        two_copies, "feat", split_axis=0, concat_axis=0, tiled=True
    ).astype(jnp.float32).reshape(local_two.shape)
    return (hidden_two[None], grad_one, grad_two)


def solution(mesh):
    return jax.shard_map(
        on_device,
        mesh=mesh,
        in_specs=(
            P("rep", "feat", None),
            P("rep", None, None),
            P(None, "feat", None),
            P(),
            P("rep", "feat", None, None),
            P("rep", "feat", None),
            P("rep", None, "feat"),
            P("rep", "feat", None),
        ),
        out_specs=(P("rep", "feat", None), P(None, "feat", None), P()),
        check_vma=False,
    )
```
